512 devices in a mesh: storey: 32 (over x_hi, z), plate: 16 (over x_lo, y, core).
Axes of the slice: x: 4 (x_hi: 2, x_lo: 2; x = x_hi * 2 + x_lo), y: 4, z: 16, core: 2. Of those that a mesh axis runs over, the one named last changes fastest.
Arguments:
- load: float32 [4096, 8192], P('storey', 'plate'), may hold values from -6 to 6
- disp: float32 [4096, 8192], P('storey', 'plate'), may hold values from -2 to 2
- mass: float32 [4096, 8192], P('storey', 'plate'), may hold values from 0.05 to 0.5
- wall_class: int32 [4096, 8192], P('storey', 'plate'), may hold values from 0 to 3
- class_stiff: float32 [4], replicated, may hold values from 0.5 to 2
- damper_map: int32 [4096, 8192], P('storey', 'plate'), may hold values from 0 to 63
- damper_coef: float32 [2048], P('storey'), may hold values from 0.2 to 2
- band_tile: float32 [16384, 8192], P('storey', 'plate')
- panel_store: float32 [16384, 8192], P('storey', 'plate')
- owner: int32 [32], P('storey'), may hold values from 0 to 15
- node_index: int32 [32, 512], P('storey', 'plate'), may hold values from 0 to 65535, as said below
Outputs:
- new_disp: float32 [4096, 8192], P('storey', 'plate')
- adjoint: float32 [4096, 8192], P('storey', 'plate')
- shear: float32 [4096], P('storey')
- grads: float32 [2048], P('storey')
The draws below stay inside these ranges and needn't reach their ends.
Inputs may be any that keep to these rules, and one draw needn't show every extreme that they name: `node_index`: the 32 nodes of one plate block of a group lie in distinct rows of the block, each given as row * 512 + column within the block.
All inputs are finite; a program needn't handle non-finite values.
Results may differ from the reference program's by a relative error of at most 0.0003.
Values sent between devices are 32-bit elements; how exact they have to be, the bound alone decides.
No kernel may reach another device: no remote copies, remote signals or barrier semaphores. Data moves between devices by JAX's collectives and lax.ppermute only.
A program may use at most 64 MiB of HBM per device.

```python
import math
import jax
import jax.numpy as jnp
from jax import lax

HC = 128
PC = 512
NODES_DEV = 32
DAMP_DEV = 64
CLASSES = 4
ITERS = 6
GROUPS = 32
NH = 4096
NP = 8192
DP = 512
DAMPERS = 2048
N_PLATE = 16


def dominant_blocks(key, rows, cols, order, centre, spread):
    first, second = jax.random.split(key)
    local_row = lax.broadcasted_iota(jnp.int32, (rows, cols), 0) % order
    local_col = lax.broadcasted_iota(jnp.int32, (rows, cols), 1) % order
    off = jax.random.normal(first, (rows, cols), jnp.float32) * (spread / math.sqrt(order))
    main = centre * (1.0 + 0.2 * jax.random.uniform(second, (rows, cols), jnp.float32, -1.0, 1.0))
    return jnp.where(local_row == local_col, main, off)


def draw_band_tile(key, part):
    return dominant_blocks(jax.random.fold_in(key, 11), GROUPS * PC, NP, PC, 0.5, 0.25)


def draw_panel_store(key, part):
    return dominant_blocks(jax.random.fold_in(key, 23), GROUPS * DP, N_PLATE * DP, DP, 0.08, 0.12)


def draw_node_index(key, part):
    first, second = jax.random.split(jax.random.fold_in(key, 37))
    span = HC // NODES_DEV
    column = lax.broadcasted_iota(jnp.int32, (GROUPS, DP), 1)
    group = lax.broadcasted_iota(jnp.int32, (GROUPS, DP), 0)
    which = column % NODES_DEV
    row = which * span + jax.random.randint(first, (GROUPS, DP), 0, span, jnp.int32)
    col = jax.random.randint(second, (GROUPS, DP), 0, PC, jnp.int32)
    index = row * PC + col
    index = jnp.where((group == 0) & (column == 0), 0, index)
    index = jnp.where((group == 0) & (column == NODES_DEV - 1), HC * PC - 1, index)
    return index.astype(jnp.int32)


def set_ends(array, stream_key, least, top_value):
    dims = array.shape
    spot = [jax.random.randint(jax.random.fold_in(stream_key, axis), (), 0, dims[axis]) for axis in range(len(dims))]
    array = array.at[tuple(spot)].set(least)
    longest = dims.index(max(dims))
    spot[longest] = (spot[longest] + 1) % dims[longest]
    return array.at[tuple(spot)].set(top_value)


def block_scale(rng, extent, pieces, low, high):
    def one(axis_at, shards_of):
        heights = jax.random.uniform(jax.random.fold_in(jax.random.fold_in(rng, 6), axis_at), (shards_of,), jnp.float32, low / len(pieces), high / len(pieces))
        return jnp.repeat(jnp.exp(heights), extent[axis_at] // shards_of).reshape((-1,) + (1,) * (len(extent) - axis_at - 1))

    factor_of = one(*pieces[0])
    for cut in pieces[1:]:
        factor_of = factor_of * one(*cut)
    return factor_of


def bell_draw(rng, extent, scale, bound, shards=(), kind=jnp.bfloat16):
    array = jax.random.normal(rng, extent, jnp.float32) * scale
    if len(shards) > 0:
        array = block_scale(rng, extent, shards, -0.22, 0.18) * array
    return jnp.clip(array, min=-bound, max=bound).astype(kind)


def setup_inputs(seed: int = 0) -> dict:
    seeds = jax.random.split(jax.random.key(seed), 12)
    load = bell_draw(seeds[0], (NH, NP), 1.0, 6.0, ((0, 32), (1, 16)), jnp.float32)
    disp = bell_draw(seeds[1], (NH, NP), 0.3, 2.0, ((0, 32), (1, 16)), jnp.float32)
    mass = jnp.clip(jnp.exp(math.log(0.5) - 2.3025851 * jax.random.uniform(seeds[2], (NH, NP), jnp.float32) ** block_scale(seeds[2], (NH, NP), ((0, 32), (1, 16)), -0.2, 0.2)), 0.05, 0.5)
    wall_class = set_ends(jax.random.randint(seeds[3], (NH, NP), 0, CLASSES), jax.random.fold_in(seeds[3], 1), 0, CLASSES - 1).astype(jnp.int32)
    class_stiff = jnp.clip(jnp.exp(jax.random.uniform(seeds[4], (CLASSES,), jnp.float32, math.log(0.5), math.log(2.0))), 0.5, 2.0)
    damper_map = set_ends(jax.random.randint(seeds[5], (NH, NP), 0, DAMP_DEV), jax.random.fold_in(seeds[5], 1), 0, DAMP_DEV - 1).astype(jnp.int32)
    damper_coef = jnp.clip(jnp.exp(math.log(2.0) - 2.3025851 * jax.random.uniform(seeds[6], (DAMPERS,), jnp.float32) ** block_scale(seeds[6], (DAMPERS,), ((0, 32),), -0.2, 0.2)), 0.2, 2.0)
    band_tile = draw_band_tile(jax.random.fold_in(seeds[11], 71), 0)
    panel_store = draw_panel_store(jax.random.fold_in(seeds[11], 71), 0)
    owner = set_ends(jax.random.randint(seeds[9], (GROUPS,), 0, N_PLATE), jax.random.fold_in(seeds[9], 1), 0, N_PLATE - 1).astype(jnp.int32)
    node_index = draw_node_index(jax.random.fold_in(seeds[11], 71), 0)
    return {"load": load, "disp": disp, "mass": mass, "wall_class": wall_class, "class_stiff": class_stiff, "damper_map": damper_map, "damper_coef": damper_coef, "band_tile": band_tile, "panel_store": panel_store, "owner": owner, "node_index": node_index}


KF = 5.0 / 9.0
CM = 2.16
CD = 1.1
HIGH = lax.Precision.HIGHEST

def neighbours(field):
    padded = jnp.pad(field, 1)
    return padded[2:, 1:-1] + padded[:-2, 1:-1] + padded[1:-1, 2:] + padded[1:-1, :-2]

def reference(load, disp, mass, wall_class, class_stiff, damper_map, damper_coef, band_tile, panel_store, owner, node_index):
    row_ids = jnp.arange(NH, dtype=jnp.int32)
    group = row_ids // HC
    stiff = KF * class_stiff[wall_class]
    inertia = CM * mass
    damping = CD * damper_coef[group[:, None] * DAMP_DEV + damper_map]
    diag = 4.0 * stiff + inertia + damping
    tiles = band_tile.reshape(GROUPS, PC, N_PLATE, PC)
    panels = panel_store.reshape(GROUPS, DP, N_PLATE, DP)
    chosen = jnp.take_along_axis(panels, owner[:, None, None, None].astype(jnp.int32), axis=2)[:, :, 0, :]
    plate_of = jnp.arange(DP, dtype=jnp.int32) // NODES_DEV
    node_row = jnp.arange(GROUPS, dtype=jnp.int32)[:, None] * HC + node_index // PC
    node_col = plate_of[None, :] * PC + node_index % PC

    def correct(resid, transpose):
        scaled = (resid / diag).reshape(GROUPS, HC, N_PLATE, PC)
        form = 'shpc,sdpc->shpd' if transpose else 'shpc,scpd->shpd'
        result = jnp.einsum(form, scaled, tiles, precision=HIGH).reshape(NH, NP)
        values = resid[node_row, node_col]
        form_two = 'sji,sj->si' if transpose else 'sij,sj->si'
        coarse = jnp.einsum(form_two, chosen, values, precision=HIGH)
        return result.at[node_row, node_col].add(coarse)
    new_disp = disp
    resid = load - (diag * new_disp - stiff * neighbours(new_disp))
    for step in range(ITERS):
        new_disp = new_disp + correct(resid, False)
        if step < ITERS - 1:
            resid = load - (diag * new_disp - stiff * neighbours(new_disp))
    force = 8.0 / math.sqrt(NP * NH) * lax.optimization_barrier(jnp.sum(inertia * new_disp, axis=1))
    shear = jnp.cumsum(force[::-1])[::-1]
    drift = jnp.cumsum(shear) / NH
    target = inertia * drift[:, None]
    adjoint = jnp.zeros_like(load)
    resid = target
    for step in range(ITERS):
        adjoint = adjoint + correct(resid, True)
        if step < ITERS - 1:
            resid = target - (diag * adjoint - neighbours(stiff * adjoint))
    product = (adjoint * new_disp).reshape(-1)
    ids = (group[:, None] * DAMP_DEV + damper_map).reshape(-1)
    sums = jax.ops.segment_sum(product, ids, num_segments=DAMPERS)
    grads = -CD * 64.0 / math.sqrt(HC * NP / DAMP_DEV) * sums
    return (new_disp, adjoint, shear, grads)
```

```python
import math

import jax
import jax.numpy as jnp
from jax import lax
from jax.sharding import PartitionSpec as P

ITERS = 6


KF = 5.0 / 9.0
CM = 2.16
CD = 1.1
HIGH = lax.Precision.HIGHEST


def with_halo(x, sides, width):
    for axis, dim in sides:
        devices, length = (lax.axis_size(axis), x.shape[dim])
        up = [(i, (i + 1) % devices) for i in range(devices - 1)]
        down = [(j, i) for i, j in up]
        last = lax.slice_in_dim(x, length - width, length, axis=dim)
        first = lax.slice_in_dim(x, 0, width, axis=dim)
        before = lax.ppermute(last, axis, up)
        after = lax.ppermute(first, axis, down)
        x = jnp.concatenate([before, x, after], axis=dim)
    return x


def by_shift(value, axis):
    devices = lax.axis_size(axis)
    got = [value]
    for shift in range(1, devices):
        pairs = [(a, (a + shift) % devices) for a in range(devices)]
        got.append(lax.ppermute(value, axis, pairs))
    return jnp.stack(got)


def to_source_order(stacked, axis):
    devices, position = (lax.axis_size(axis), lax.axis_index(axis))
    order = (position - jnp.arange(devices, dtype=jnp.int32)) % devices
    return jnp.take(stacked, order, axis=0)


def gather_all(value, axis):
    return to_source_order(by_shift(value, axis), axis)


def sum_all(value, axis):
    return jnp.sum(gather_all(value, axis), axis=0)


def neighbours(field):
    padded = with_halo(field, (("storey", 0), ("plate", 1)), 1)
    return padded[2:, 1:-1] + padded[:-2, 1:-1] + padded[1:-1, 2:] + padded[1:-1, :-2]


def damper_lookup(ids, coef):
    rows, cols = ids.shape
    blocks = ids.reshape(rows // 16, 16, cols)
    labels = jnp.arange(coef.shape[0], dtype=jnp.int32)

    def one_block(block):
        match = block[None, :, :] == labels[:, None, None]
        return jnp.sum(jnp.where(match, coef[:, None, None], 0.0), axis=0)

    return lax.map(one_block, blocks).reshape(rows, cols)


def damper_totals(ids, values, count):
    rows, cols = ids.shape
    labels = jnp.arange(count, dtype=jnp.int32)

    def one_block(pair):
        match = pair[0][None, :, :] == labels[:, None, None]
        return jnp.sum(jnp.where(match, pair[1][None, :, :], 0.0), axis=(1, 2))

    parts = lax.map(
        one_block, (ids.reshape(rows // 16, 16, cols), values.reshape(rows // 16, 16, cols))
    )
    return jnp.sum(parts, axis=0)


def panel_slabs(panel_store, owner, nodes):
    n_plate = lax.axis_size("plate")
    here = lax.axis_index("plate")
    mine = here == owner
    rows_of = panel_store.reshape(n_plate, nodes, -1)
    cols_of = jnp.swapaxes(panel_store.reshape(-1, n_plate, nodes), 0, 1)
    cols_of = jnp.swapaxes(cols_of, 1, 2)

    def fetch(slabs):
        got = [jnp.where(mine, slabs[here], 0.0)]
        for shift in range(1, n_plate):
            pairs = [(a, (a + shift) % n_plate) for a in range(n_plate)]
            target = (here + shift) % n_plate
            got.append(lax.ppermute(jnp.where(mine, slabs[target], 0.0), "plate", pairs))
        total = got[0]
        for piece in got[1:]:
            total = total + piece
        order = (here - jnp.arange(n_plate, dtype=jnp.int32)) % n_plate
        total = total.reshape(nodes, n_plate, nodes)
        return jnp.take(total, order, axis=1).reshape(nodes, n_plate * nodes)

    return fetch(rows_of), fetch(cols_of)


def on_device(
    load,
    disp,
    mass,
    wall_class,
    class_stiff,
    damper_map,
    damper_coef,
    band_tile,
    panel_store,
    owner,
    node_index,
):
    rows, cols = load.shape
    n_storey = lax.axis_size("storey")
    n_plate = lax.axis_size("plate")
    total_rows = rows * n_storey
    total_cols = cols * n_plate
    nodes = node_index.shape[1]
    stiff = jnp.zeros_like(load)
    for level in range(class_stiff.shape[0]):
        stiff = stiff + jnp.where(wall_class == level, class_stiff[level], 0.0)
    stiff = KF * stiff
    inertia = CM * mass
    damping = CD * damper_lookup(damper_map, damper_coef)
    diag = 4.0 * stiff + inertia + damping
    places = node_index[0]
    row_slab, col_slab = panel_slabs(panel_store, owner[0], nodes)

    def correct(resid, transpose):
        scaled = resid / diag
        if transpose:
            result = lax.dot_general(scaled, band_tile, (((1,), (1,)), ((), ())), precision=HIGH)
        else:
            result = jnp.dot(scaled, band_tile, precision=HIGH)
        picked = resid.reshape(-1)[places]
        values = by_shift(picked, "plate").reshape(-1)
        slab = col_slab if transpose else row_slab
        mine = jnp.dot(slab, values, precision=HIGH)
        return result.reshape(-1).at[places].add(mine).reshape(rows, cols)

    new_disp = disp
    resid = load - (diag * new_disp - stiff * neighbours(new_disp))
    for step in range(ITERS):
        new_disp = new_disp + correct(resid, False)
        if step < ITERS - 1:
            resid = load - (diag * new_disp - stiff * neighbours(new_disp))
    partial_force = jnp.sum(inertia * new_disp, axis=1)
    force = sum_all(partial_force, "plate") * (8.0 / math.sqrt(total_cols * total_rows))
    every_force = gather_all(force, "storey").reshape(-1)
    every_shear = jnp.cumsum(every_force[::-1])[::-1]
    every_drift = jnp.cumsum(every_shear) / total_rows
    here_storey = lax.axis_index("storey")
    shear = lax.dynamic_slice_in_dim(every_shear, here_storey * rows, rows)
    drift = lax.dynamic_slice_in_dim(every_drift, here_storey * rows, rows)
    target = inertia * drift[:, None]
    adjoint = jnp.zeros_like(load)
    resid = target
    for step in range(ITERS):
        adjoint = adjoint + correct(resid, True)
        if step < ITERS - 1:
            resid = target - (diag * adjoint - neighbours(stiff * adjoint))
    partial_sums = damper_totals(damper_map, adjoint * new_disp, damper_coef.shape[0])
    sums = sum_all(partial_sums, "plate")
    grads = -CD * 64.0 / math.sqrt(rows * total_cols / damper_coef.shape[0]) * sums
    return (new_disp, adjoint, shear, grads)


def solution(mesh):
    return jax.shard_map(
        on_device,
        mesh=mesh,
        in_specs=(
            P("storey", "plate"),
            P("storey", "plate"),
            P("storey", "plate"),
            P("storey", "plate"),
            P(),
            P("storey", "plate"),
            P("storey"),
            P("storey", "plate"),
            P("storey", "plate"),
            P("storey"),
            P("storey", "plate"),
        ),
        out_specs=(P("storey", "plate"), P("storey", "plate"), P("storey"), P("storey")),
        check_vma=False,
    )
```

```python
import math

import jax
import jax.numpy as jnp
from jax import lax
from jax.sharding import PartitionSpec as P

ITERS = 6


KF = 5.0 / 9.0
CM = 2.16
CD = 1.1
HIGH = lax.Precision.HIGHEST


def with_halo(x, sides, width):
    for axis, dim in sides:
        devices, length = (lax.axis_size(axis), x.shape[dim])
        up = [(i, (i + 1) % devices) for i in range(devices - 1)]
        down = [(j, i) for i, j in up]
        last = lax.slice_in_dim(x, length - width, length, axis=dim)
        first = lax.slice_in_dim(x, 0, width, axis=dim)
        before = lax.ppermute(last, axis, up)
        after = lax.ppermute(first, axis, down)
        x = jnp.concatenate([before, x, after], axis=dim)
    return x


def gather_all(value, axis):
    devices = lax.axis_size(axis)
    spread = jnp.broadcast_to(value[None], (devices,) + value.shape)
    return lax.all_to_all(spread, axis, 0, 0, tiled=False)


def sum_all(value, axis):
    return jnp.sum(gather_all(value, axis), axis=0)


def neighbours(field):
    padded = with_halo(field, (("storey", 0), ("plate", 1)), 1)
    return padded[2:, 1:-1] + padded[:-2, 1:-1] + padded[1:-1, 2:] + padded[1:-1, :-2]


def damper_lookup(ids, coef):
    rows, cols = ids.shape
    blocks = ids.reshape(rows // 16, 16, cols)
    labels = jnp.arange(coef.shape[0], dtype=jnp.int32)

    def one_block(block):
        match = block[None, :, :] == labels[:, None, None]
        return jnp.sum(jnp.where(match, coef[:, None, None], 0.0), axis=0)

    return lax.map(one_block, blocks).reshape(rows, cols)


def damper_totals(ids, values, count):
    rows, cols = ids.shape
    labels = jnp.arange(count, dtype=jnp.int32)

    def one_block(pair):
        match = pair[0][None, :, :] == labels[:, None, None]
        return jnp.sum(jnp.where(match, pair[1][None, :, :], 0.0), axis=(1, 2))

    parts = lax.map(
        one_block, (ids.reshape(rows // 16, 16, cols), values.reshape(rows // 16, 16, cols))
    )
    return jnp.sum(parts, axis=0)


def panel_slabs(panel_store, owner, nodes):
    n_plate = lax.axis_size("plate")
    mine = lax.axis_index("plate") == owner
    rows_of = panel_store.reshape(n_plate, nodes, -1)
    cols_of = jnp.swapaxes(panel_store.reshape(-1, n_plate, nodes), 0, 1)
    cols_of = jnp.swapaxes(cols_of, 1, 2)

    def fetch(slabs):
        sent = jnp.where(mine, slabs, 0.0)
        return jnp.sum(lax.all_to_all(sent, "plate", 0, 0, tiled=False), axis=0)

    return fetch(rows_of), fetch(cols_of)


def on_device(
    load,
    disp,
    mass,
    wall_class,
    class_stiff,
    damper_map,
    damper_coef,
    band_tile,
    panel_store,
    owner,
    node_index,
):
    rows, cols = load.shape
    n_storey = lax.axis_size("storey")
    n_plate = lax.axis_size("plate")
    total_rows = rows * n_storey
    total_cols = cols * n_plate
    nodes = node_index.shape[1]
    stiff = jnp.zeros_like(load)
    for level in range(class_stiff.shape[0]):
        stiff = stiff + jnp.where(wall_class == level, class_stiff[level], 0.0)
    stiff = KF * stiff
    inertia = CM * mass
    damping = CD * damper_lookup(damper_map, damper_coef)
    diag = 4.0 * stiff + inertia + damping
    places = node_index[0]
    row_slab, col_slab = panel_slabs(panel_store, owner[0], nodes)

    def correct(resid, transpose):
        scaled = resid / diag
        if transpose:
            result = lax.dot_general(scaled, band_tile, (((1,), (1,)), ((), ())), precision=HIGH)
        else:
            result = jnp.dot(scaled, band_tile, precision=HIGH)
        picked = resid.reshape(-1)[places]
        values = gather_all(picked, "plate").reshape(-1)
        slab = col_slab if transpose else row_slab
        mine = jnp.dot(slab, values, precision=HIGH)
        return result.reshape(-1).at[places].add(mine).reshape(rows, cols)

    new_disp = disp
    resid = load - (diag * new_disp - stiff * neighbours(new_disp))
    for step in range(ITERS):
        new_disp = new_disp + correct(resid, False)
        if step < ITERS - 1:
            resid = load - (diag * new_disp - stiff * neighbours(new_disp))
    partial_force = jnp.sum(inertia * new_disp, axis=1)
    force = sum_all(partial_force, "plate") * (8.0 / math.sqrt(total_cols * total_rows))
    every_force = gather_all(force, "storey").reshape(-1)
    every_shear = jnp.cumsum(every_force[::-1])[::-1]
    every_drift = jnp.cumsum(every_shear) / total_rows
    here_storey = lax.axis_index("storey")
    shear = lax.dynamic_slice_in_dim(every_shear, here_storey * rows, rows)
    drift = lax.dynamic_slice_in_dim(every_drift, here_storey * rows, rows)
    target = inertia * drift[:, None]
    adjoint = jnp.zeros_like(load)
    resid = target
    for step in range(ITERS):
        adjoint = adjoint + correct(resid, True)
        if step < ITERS - 1:
            resid = target - (diag * adjoint - neighbours(stiff * adjoint))
    partial_sums = damper_totals(damper_map, adjoint * new_disp, damper_coef.shape[0])
    sums = sum_all(partial_sums, "plate")
    grads = -CD * 64.0 / math.sqrt(rows * total_cols / damper_coef.shape[0]) * sums
    return (new_disp, adjoint, shear, grads)


def solution(mesh):
    return jax.shard_map(
        on_device,
        mesh=mesh,
        in_specs=(
            P("storey", "plate"),
            P("storey", "plate"),
            P("storey", "plate"),
            P("storey", "plate"),
            P(),
            P("storey", "plate"),
            P("storey"),
            P("storey", "plate"),
            P("storey", "plate"),
            P("storey"),
            P("storey", "plate"),
        ),
        out_specs=(P("storey", "plate"), P("storey", "plate"), P("storey"), P("storey")),
        check_vma=False,
    )
```

```python
import math

import jax
import jax.numpy as jnp
from jax import lax
from jax.sharding import PartitionSpec as P

ITERS = 6


KF = 5.0 / 9.0
CM = 2.16
CD = 1.1
HIGH = lax.Precision.HIGHEST


def shifted(x, axis, dim, toward):
    devices, length = (lax.axis_size(axis), x.shape[dim])
    if toward > 0:
        pairs = [(i, i + 1) for i in range(devices - 1)]
        edge = lax.slice_in_dim(x, length - 1, length, axis=dim)
    else:
        pairs = [(i + 1, i) for i in range(devices - 1)]
        edge = lax.slice_in_dim(x, 0, 1, axis=dim)
    return lax.ppermute(edge, axis, pairs)


def gather_all(value, axis):
    devices = lax.axis_size(axis)
    spread = jnp.broadcast_to(value[None], (devices,) + value.shape)
    return lax.all_to_all(spread, axis, 0, 0, tiled=False)


def sum_all(value, axis):
    return jnp.sum(gather_all(value, axis), axis=0)


def neighbours(field):
    above = shifted(field, "storey", 0, 1)
    below = shifted(field, "storey", 0, -1)
    left = shifted(field, "plate", 1, 1)
    right = shifted(field, "plate", 1, -1)
    vertical = jnp.concatenate([above, field[:-1]], axis=0) + jnp.concatenate([field[1:], below], axis=0)
    horizontal = jnp.concatenate([left, field[:, :-1]], axis=1) + jnp.concatenate([field[:, 1:], right], axis=1)
    return vertical + horizontal


def damper_lookup(ids, coef):
    rows, cols = ids.shape
    blocks = ids.reshape(rows // 16, 16, cols)
    labels = jnp.arange(coef.shape[0], dtype=jnp.int32)

    def one_block(block):
        match = block[None, :, :] == labels[:, None, None]
        return jnp.sum(jnp.where(match, coef[:, None, None], 0.0), axis=0)

    return lax.map(one_block, blocks).reshape(rows, cols)


def damper_totals(ids, values, count):
    rows, cols = ids.shape
    labels = jnp.arange(count, dtype=jnp.int32)

    def one_block(pair):
        match = pair[0][None, :, :] == labels[:, None, None]
        return jnp.sum(jnp.where(match, pair[1][None, :, :], 0.0), axis=(1, 2))

    parts = lax.map(
        one_block, (ids.reshape(rows // 16, 16, cols), values.reshape(rows // 16, 16, cols))
    )
    return jnp.sum(parts, axis=0)


def panel_slabs(panel_store, owner, nodes):
    n_plate = lax.axis_size("plate")
    mine = lax.axis_index("plate") == owner
    rows_of = panel_store.reshape(n_plate, nodes, -1)
    cols_of = jnp.swapaxes(panel_store.reshape(-1, n_plate, nodes), 0, 1)
    cols_of = jnp.swapaxes(cols_of, 1, 2)

    both = jnp.concatenate([rows_of, cols_of], axis=1)
    sent = jnp.where(mine, both, 0.0)
    got = jnp.sum(lax.all_to_all(sent, "plate", 0, 0, tiled=False), axis=0)
    return got[:nodes], got[nodes:]


def on_device(
    load,
    disp,
    mass,
    wall_class,
    class_stiff,
    damper_map,
    damper_coef,
    band_tile,
    panel_store,
    owner,
    node_index,
):
    rows, cols = load.shape
    n_storey = lax.axis_size("storey")
    n_plate = lax.axis_size("plate")
    total_rows = rows * n_storey
    total_cols = cols * n_plate
    nodes = node_index.shape[1]
    stiff = jnp.zeros_like(load)
    for level in range(class_stiff.shape[0]):
        stiff = stiff + jnp.where(wall_class == level, class_stiff[level], 0.0)
    stiff = KF * stiff
    inertia = CM * mass
    damping = CD * damper_lookup(damper_map, damper_coef)
    diag = 4.0 * stiff + inertia + damping
    places = node_index[0]
    row_slab, col_slab = panel_slabs(panel_store, owner[0], nodes)

    def correct(resid, transpose):
        scaled = resid / diag
        if transpose:
            result = lax.dot_general(scaled, band_tile, (((1,), (1,)), ((), ())), precision=HIGH)
        else:
            result = jnp.dot(scaled, band_tile, precision=HIGH)
        picked = resid.reshape(-1)[places]
        values = gather_all(picked, "plate").reshape(-1)
        slab = col_slab if transpose else row_slab
        mine = jnp.dot(slab, values, precision=HIGH)
        return result.reshape(-1).at[places].add(mine).reshape(rows, cols)

    new_disp = disp
    resid = load - (diag * new_disp - stiff * neighbours(new_disp))
    for step in range(ITERS):
        new_disp = new_disp + correct(resid, False)
        if step < ITERS - 1:
            resid = load - (diag * new_disp - stiff * neighbours(new_disp))
    partial_force = jnp.sum(inertia * new_disp, axis=1)
    force = sum_all(partial_force, "plate") * (8.0 / math.sqrt(total_cols * total_rows))
    every_force = gather_all(force, "storey").reshape(-1)
    every_shear = jnp.cumsum(every_force[::-1])[::-1]
    every_drift = jnp.cumsum(every_shear) / total_rows
    here_storey = lax.axis_index("storey")
    shear = lax.dynamic_slice_in_dim(every_shear, here_storey * rows, rows)
    drift = lax.dynamic_slice_in_dim(every_drift, here_storey * rows, rows)
    target = inertia * drift[:, None]
    adjoint = jnp.zeros_like(load)
    resid = target
    for step in range(ITERS):
        adjoint = adjoint + correct(resid, True)
        if step < ITERS - 1:
            resid = target - (diag * adjoint - neighbours(stiff * adjoint))
    partial_sums = damper_totals(damper_map, adjoint * new_disp, damper_coef.shape[0])
    sums = sum_all(partial_sums, "plate")
    grads = -CD * 64.0 / math.sqrt(rows * total_cols / damper_coef.shape[0]) * sums
    return (new_disp, adjoint, shear, grads)


def solution(mesh):
    return jax.shard_map(
        on_device,
        mesh=mesh,
        in_specs=(
            P("storey", "plate"),
            P("storey", "plate"),
            P("storey", "plate"),
            P("storey", "plate"),
            P(),
            P("storey", "plate"),
            P("storey"),
            P("storey", "plate"),
            P("storey", "plate"),
            P("storey"),
            P("storey", "plate"),
        ),
        out_specs=(P("storey", "plate"), P("storey", "plate"), P("storey"), P("storey")),
        check_vma=False,
    )
```

```python
import math

import jax
import jax.numpy as jnp
from jax import lax
from jax.sharding import PartitionSpec as P

ITERS = 6


KF = 5.0 / 9.0
CM = 2.16
CD = 1.1
HIGH = lax.Precision.HIGHEST


def shifted(x, axis, dim, toward):
    devices, length = (lax.axis_size(axis), x.shape[dim])
    if toward > 0:
        pairs = [(i, i + 1) for i in range(devices - 1)]
        edge = lax.slice_in_dim(x, length - 1, length, axis=dim)
    else:
        pairs = [(i + 1, i) for i in range(devices - 1)]
        edge = lax.slice_in_dim(x, 0, 1, axis=dim)
    return lax.ppermute(edge, axis, pairs)


def gather_all(value, axis):
    devices = lax.axis_size(axis)
    spread = jnp.broadcast_to(value[None], (devices,) + value.shape)
    return lax.all_to_all(spread, axis, 0, 0, tiled=False)


def sum_all(value, axis):
    return jnp.sum(gather_all(value, axis), axis=0)


def around(field, above, below, left, right):
    vertical = jnp.concatenate([above, field[:-1]], axis=0) + jnp.concatenate([field[1:], below], axis=0)
    horizontal = jnp.concatenate([left, field[:, :-1]], axis=1) + jnp.concatenate([field[:, 1:], right], axis=1)
    return vertical + horizontal


def neighbours(field):
    above = shifted(field, "storey", 0, 1)
    below = shifted(field, "storey", 0, -1)
    left = shifted(field, "plate", 1, 1)
    right = shifted(field, "plate", 1, -1)
    return around(field, above, below, left, right)


def edge_panels(row_slab, col_slab, places, stiff):
    rows, cols = stiff.shape
    node_row = places // cols
    node_col = places % cols
    at_last = (node_col == cols - 1)[:, None]
    at_first = (node_col == 0)[:, None]
    stiff_last = stiff[node_row, cols - 1][:, None]
    stiff_first = stiff[node_row, 0][:, None]

    def spread(picked):
        return jnp.zeros((rows, picked.shape[1]), picked.dtype).at[node_row].add(picked)

    to_right = jnp.stack([spread(jnp.where(at_last, row_slab, 0.0)), spread(jnp.where(at_last, stiff_last * col_slab, 0.0))])
    to_left = jnp.stack([spread(jnp.where(at_first, row_slab, 0.0)), spread(jnp.where(at_first, stiff_first * col_slab, 0.0))])
    n_plate = lax.axis_size("plate")
    from_left = lax.ppermute(to_right, "plate", [(i, i + 1) for i in range(n_plate - 1)])
    from_right = lax.ppermute(to_left, "plate", [(i + 1, i) for i in range(n_plate - 1)])
    return from_left, from_right


def damper_lookup(ids, coef):
    rows, cols = ids.shape
    blocks = ids.reshape(rows // 16, 16, cols)
    labels = jnp.arange(coef.shape[0], dtype=jnp.int32)

    def one_block(block):
        match = block[None, :, :] == labels[:, None, None]
        return jnp.sum(jnp.where(match, coef[:, None, None], 0.0), axis=0)

    return lax.map(one_block, blocks).reshape(rows, cols)


def damper_totals(ids, values, count):
    rows, cols = ids.shape
    labels = jnp.arange(count, dtype=jnp.int32)

    def one_block(pair):
        match = pair[0][None, :, :] == labels[:, None, None]
        return jnp.sum(jnp.where(match, pair[1][None, :, :], 0.0), axis=(1, 2))

    parts = lax.map(
        one_block, (ids.reshape(rows // 16, 16, cols), values.reshape(rows // 16, 16, cols))
    )
    return jnp.sum(parts, axis=0)


def panel_slabs(panel_store, owner, nodes):
    n_plate = lax.axis_size("plate")
    mine = lax.axis_index("plate") == owner
    rows_of = panel_store.reshape(n_plate, nodes, -1)
    cols_of = jnp.swapaxes(panel_store.reshape(-1, n_plate, nodes), 0, 1)
    cols_of = jnp.swapaxes(cols_of, 1, 2)

    both = jnp.concatenate([rows_of, cols_of], axis=1)
    sent = jnp.where(mine, both, 0.0)
    got = jnp.sum(lax.all_to_all(sent, "plate", 0, 0, tiled=False), axis=0)
    return got[:nodes], got[nodes:]


def on_device(
    load,
    disp,
    mass,
    wall_class,
    class_stiff,
    damper_map,
    damper_coef,
    band_tile,
    panel_store,
    owner,
    node_index,
):
    rows, cols = load.shape
    n_storey = lax.axis_size("storey")
    n_plate = lax.axis_size("plate")
    total_rows = rows * n_storey
    total_cols = cols * n_plate
    nodes = node_index.shape[1]
    stiff = jnp.zeros_like(load)
    for level in range(class_stiff.shape[0]):
        stiff = stiff + jnp.where(wall_class == level, class_stiff[level], 0.0)
    stiff = KF * stiff
    inertia = CM * mass
    damping = CD * damper_lookup(damper_map, damper_coef)
    diag = 4.0 * stiff + inertia + damping
    places = node_index[0]
    row_slab, col_slab = panel_slabs(panel_store, owner[0], nodes)

    from_left, from_right = edge_panels(row_slab, col_slab, places, stiff)
    here = lax.axis_index("plate")
    has_left = here > 0
    has_right = here < n_plate - 1
    left_at = jnp.maximum(here - 1, 0)
    right_at = jnp.minimum(here + 1, n_plate - 1)

    def step(field, resid, transpose, halo_of, last, first=False):
        scaled = resid / diag
        if transpose:
            result = lax.dot_general(scaled, band_tile, (((1,), (1,)), ((), ())), precision=HIGH)
        else:
            result = jnp.dot(scaled, band_tile, precision=HIGH)
        moved = field + result
        edge = halo_of(moved)
        picked = resid.reshape(-1)[places]
        payload = jnp.concatenate([picked, edge[:, -1], edge[:, 0]])
        if first:
            payload, _ = lax.optimization_barrier((payload, row_slab))
        got = gather_all(payload, "plate")
        values = got[:, :nodes].reshape(-1)
        slab = col_slab if transpose else row_slab
        mine = jnp.dot(slab, values, precision=HIGH)
        updated = moved.reshape(-1).at[places].add(mine).reshape(rows, cols)
        if last:
            return updated, None
        which = 1 if transpose else 0
        left = got[left_at, nodes:nodes + rows] + jnp.dot(from_left[which], values, precision=HIGH)
        right = got[right_at, nodes + rows:] + jnp.dot(from_right[which], values, precision=HIGH)
        left = jnp.where(has_left, left, 0.0)[:, None]
        right = jnp.where(has_right, right, 0.0)[:, None]
        spread = halo_of(updated)
        above = shifted(spread, "storey", 0, 1)
        below = shifted(spread, "storey", 0, -1)
        return updated, around(spread, above, below, left, right)

    new_disp = disp
    resid = load - (diag * new_disp - stiff * neighbours(new_disp))
    for it in range(ITERS):
        last = it == ITERS - 1
        new_disp, near = step(new_disp, resid, False, lambda v: v, last, first=it == 0)
        if not last:
            resid = load - (diag * new_disp - stiff * near)
    partial_force = jnp.sum(inertia * new_disp, axis=1)
    force = sum_all(partial_force, "plate") * (8.0 / math.sqrt(total_cols * total_rows))
    every_force = gather_all(force, "storey").reshape(-1)
    every_shear = jnp.cumsum(every_force[::-1])[::-1]
    every_drift = jnp.cumsum(every_shear) / total_rows
    here_storey = lax.axis_index("storey")
    shear = lax.dynamic_slice_in_dim(every_shear, here_storey * rows, rows)
    drift = lax.dynamic_slice_in_dim(every_drift, here_storey * rows, rows)
    target = inertia * drift[:, None]
    adjoint = jnp.zeros_like(load)
    resid = target
    for it in range(ITERS):
        last = it == ITERS - 1
        adjoint, near = step(adjoint, resid, True, lambda v: stiff * v, last)
        if not last:
            resid = target - (diag * adjoint - near)
    partial_sums = damper_totals(damper_map, adjoint * new_disp, damper_coef.shape[0])
    sums = sum_all(partial_sums, "plate")
    grads = -CD * 64.0 / math.sqrt(rows * total_cols / damper_coef.shape[0]) * sums
    return (new_disp, adjoint, shear, grads)


def solution(mesh):
    return jax.shard_map(
        on_device,
        mesh=mesh,
        in_specs=(
            P("storey", "plate"),
            P("storey", "plate"),
            P("storey", "plate"),
            P("storey", "plate"),
            P(),
            P("storey", "plate"),
            P("storey"),
            P("storey", "plate"),
            P("storey", "plate"),
            P("storey"),
            P("storey", "plate"),
        ),
        out_specs=(P("storey", "plate"), P("storey", "plate"), P("storey"), P("storey")),
        check_vma=False,
    )
```

```python
import math

import jax
import jax.numpy as jnp
from jax import lax
from jax.sharding import PartitionSpec as P

ITERS = 6


KF = 5.0 / 9.0
CM = 2.16
CD = 1.1
HIGH = lax.Precision.HIGHEST


def shifted(x, axis, dim, toward):
    devices, length = (lax.axis_size(axis), x.shape[dim])
    if toward > 0:
        pairs = [(i, i + 1) for i in range(devices - 1)]
        edge = lax.slice_in_dim(x, length - 1, length, axis=dim)
    else:
        pairs = [(i + 1, i) for i in range(devices - 1)]
        edge = lax.slice_in_dim(x, 0, 1, axis=dim)
    return lax.ppermute(edge, axis, pairs)


def gather_all(value, axis):
    devices = lax.axis_size(axis)
    spread = jnp.broadcast_to(value[None], (devices,) + value.shape)
    return lax.all_to_all(spread, axis, 0, 0, tiled=False)


def sum_all(value, axis):
    return jnp.sum(gather_all(value, axis), axis=0)


def neighbours(field):
    above = shifted(field, "storey", 0, 1)
    below = shifted(field, "storey", 0, -1)
    left = shifted(field, "plate", 1, 1)
    right = shifted(field, "plate", 1, -1)
    vertical = jnp.concatenate([above, field[:-1]], axis=0) + jnp.concatenate([field[1:], below], axis=0)
    horizontal = jnp.concatenate([left, field[:, :-1]], axis=1) + jnp.concatenate([field[:, 1:], right], axis=1)
    return vertical + horizontal


def damper_lookup(ids, coef):
    labels = jnp.arange(coef.shape[0], dtype=jnp.int32)
    match = ids[None, :, :] == labels[:, None, None]
    return jnp.sum(jnp.where(match, coef[:, None, None], 0.0), axis=0)


def damper_totals(ids, values, count):
    labels = jnp.arange(count, dtype=jnp.int32)
    match = ids[None, :, :] == labels[:, None, None]
    return jnp.sum(jnp.where(match, values[None, :, :], 0.0), axis=(1, 2))


def panel_slabs(panel_store, owner, nodes):
    n_plate = lax.axis_size("plate")
    mine = lax.axis_index("plate") == owner
    rows_of = panel_store.reshape(n_plate, nodes, -1)
    cols_of = jnp.swapaxes(panel_store.reshape(-1, n_plate, nodes), 0, 1)
    cols_of = jnp.swapaxes(cols_of, 1, 2)

    both = jnp.concatenate([rows_of, cols_of], axis=1)
    sent = jnp.where(mine, both, 0.0)
    got = jnp.sum(lax.all_to_all(sent, "plate", 0, 0, tiled=False), axis=0)
    return got[:nodes], got[nodes:]


def on_device(
    load,
    disp,
    mass,
    wall_class,
    class_stiff,
    damper_map,
    damper_coef,
    band_tile,
    panel_store,
    owner,
    node_index,
):
    rows, cols = load.shape
    n_storey = lax.axis_size("storey")
    n_plate = lax.axis_size("plate")
    total_rows = rows * n_storey
    total_cols = cols * n_plate
    nodes = node_index.shape[1]
    stiff = jnp.zeros_like(load)
    for level in range(class_stiff.shape[0]):
        stiff = stiff + jnp.where(wall_class == level, class_stiff[level], 0.0)
    stiff = KF * stiff
    inertia = CM * mass
    damping = CD * damper_lookup(damper_map, damper_coef)
    diag = 4.0 * stiff + inertia + damping
    places = node_index[0]
    row_slab, col_slab = panel_slabs(panel_store, owner[0], nodes)

    def correct(resid, transpose, first=False):
        scaled = resid / diag
        if transpose:
            result = lax.dot_general(scaled, band_tile, (((1,), (1,)), ((), ())), precision=HIGH)
        else:
            result = jnp.dot(scaled, band_tile, precision=HIGH)
        picked = resid.reshape(-1)[places]
        if first:
            picked, _ = lax.optimization_barrier((picked, row_slab))
        values = gather_all(picked, "plate").reshape(-1)
        slab = col_slab if transpose else row_slab
        mine = jnp.dot(slab, values, precision=HIGH)
        return result.reshape(-1).at[places].add(mine).reshape(rows, cols)

    new_disp = disp
    resid = load - (diag * new_disp - stiff * neighbours(new_disp))
    for step in range(ITERS):
        new_disp = new_disp + correct(resid, False, first=step == 0)
        if step < ITERS - 1:
            resid = load - (diag * new_disp - stiff * neighbours(new_disp))
    partial_force = jnp.sum(inertia * new_disp, axis=1)
    force = sum_all(partial_force, "plate") * (8.0 / math.sqrt(total_cols * total_rows))
    every_force = gather_all(force, "storey").reshape(-1)
    every_shear = jnp.cumsum(every_force[::-1])[::-1]
    every_drift = jnp.cumsum(every_shear) / total_rows
    here_storey = lax.axis_index("storey")
    shear = lax.dynamic_slice_in_dim(every_shear, here_storey * rows, rows)
    drift = lax.dynamic_slice_in_dim(every_drift, here_storey * rows, rows)
    target = inertia * drift[:, None]
    adjoint = jnp.zeros_like(load)
    resid = target
    for step in range(ITERS):
        adjoint = adjoint + correct(resid, True)
        if step < ITERS - 1:
            resid = target - (diag * adjoint - neighbours(stiff * adjoint))
    partial_sums = damper_totals(damper_map, adjoint * new_disp, damper_coef.shape[0])
    sums = sum_all(partial_sums, "plate")
    grads = -CD * 64.0 / math.sqrt(rows * total_cols / damper_coef.shape[0]) * sums
    return (new_disp, adjoint, shear, grads)


def solution(mesh):
    return jax.shard_map(
        on_device,
        mesh=mesh,
        in_specs=(
            P("storey", "plate"),
            P("storey", "plate"),
            P("storey", "plate"),
            P("storey", "plate"),
            P(),
            P("storey", "plate"),
            P("storey"),
            P("storey", "plate"),
            P("storey", "plate"),
            P("storey"),
            P("storey", "plate"),
        ),
        out_specs=(P("storey", "plate"), P("storey", "plate"), P("storey"), P("storey")),
        check_vma=False,
    )
```

```python
import math

import jax
import jax.numpy as jnp
from jax import lax
from jax.sharding import PartitionSpec as P

ITERS = 6


KF = 5.0 / 9.0
CM = 2.16
CD = 1.1
HIGH = lax.Precision.HIGHEST


def shifted(x, axis, dim, toward):
    devices, length = (lax.axis_size(axis), x.shape[dim])
    if toward > 0:
        pairs = [(i, i + 1) for i in range(devices - 1)]
        edge = lax.slice_in_dim(x, length - 1, length, axis=dim)
    else:
        pairs = [(i + 1, i) for i in range(devices - 1)]
        edge = lax.slice_in_dim(x, 0, 1, axis=dim)
    return lax.ppermute(edge, axis, pairs)


def gather_all(value, axis):
    devices = lax.axis_size(axis)
    spread = jnp.broadcast_to(value[None], (devices,) + value.shape)
    return lax.all_to_all(spread, axis, 0, 0, tiled=False)


def sum_all(value, axis):
    return jnp.sum(gather_all(value, axis), axis=0)


def neighbours(field):
    above = shifted(field, "storey", 0, 1)
    below = shifted(field, "storey", 0, -1)
    left = shifted(field, "plate", 1, 1)
    right = shifted(field, "plate", 1, -1)
    vertical = jnp.concatenate([above, field[:-1]], axis=0) + jnp.concatenate([field[1:], below], axis=0)
    horizontal = jnp.concatenate([left, field[:, :-1]], axis=1) + jnp.concatenate([field[:, 1:], right], axis=1)
    return vertical + horizontal


def damper_lookup(ids, coef):
    labels = jnp.arange(coef.shape[0], dtype=jnp.int32)
    match = ids[None, :, :] == labels[:, None, None]
    return jnp.sum(jnp.where(match, coef[:, None, None], 0.0), axis=0)


def damper_totals(ids, values, count):
    labels = jnp.arange(count, dtype=jnp.int32)
    match = ids[None, :, :] == labels[:, None, None]
    return jnp.sum(jnp.where(match, values[None, :, :], 0.0), axis=(1, 2))


def panel_slabs(panel_store, owner, nodes):
    n_plate = lax.axis_size("plate")
    mine = lax.axis_index("plate") == owner
    rows_of = panel_store.reshape(n_plate, nodes, -1)
    cols_of = jnp.swapaxes(panel_store.reshape(-1, n_plate, nodes), 0, 1)
    cols_of = jnp.swapaxes(cols_of, 1, 2)

    both = jnp.concatenate([rows_of, cols_of], axis=1)
    sent = jnp.where(mine, both, 0.0)
    got = jnp.sum(lax.all_to_all(sent, "plate", 0, 0, tiled=False), axis=0)
    return got[:nodes], got[nodes:]


def on_device(
    load,
    disp,
    mass,
    wall_class,
    class_stiff,
    damper_map,
    damper_coef,
    band_tile,
    panel_store,
    owner,
    node_index,
):
    rows, cols = load.shape
    n_storey = lax.axis_size("storey")
    n_plate = lax.axis_size("plate")
    total_rows = rows * n_storey
    total_cols = cols * n_plate
    nodes = node_index.shape[1]
    stiff = jnp.zeros_like(load)
    for level in range(class_stiff.shape[0]):
        stiff = stiff + jnp.where(wall_class == level, class_stiff[level], 0.0)
    stiff = KF * stiff
    inertia = CM * mass
    damping = CD * damper_lookup(damper_map, damper_coef)
    diag = 4.0 * stiff + inertia + damping
    places = node_index[0]
    row_slab, col_slab = panel_slabs(panel_store, owner[0], nodes)

    def correct(resid, transpose, first=False):
        scaled = resid / diag
        if transpose:
            result = lax.dot_general(scaled, band_tile, (((1,), (1,)), ((), ())), precision=HIGH)
        else:
            result = jnp.dot(scaled, band_tile, precision=HIGH)
        picked = resid.reshape(-1)[places]
        if first:
            picked = picked + 0.0 * row_slab[0, 0]
        values = gather_all(picked, "plate").reshape(-1)
        slab = col_slab if transpose else row_slab
        mine = jnp.dot(slab, values, precision=HIGH)
        return result.reshape(-1).at[places].add(mine).reshape(rows, cols)

    new_disp = disp
    resid = load - (diag * new_disp - stiff * neighbours(new_disp))
    for step in range(ITERS):
        new_disp = new_disp + correct(resid, False, first=step == 0)
        if step < ITERS - 1:
            resid = load - (diag * new_disp - stiff * neighbours(new_disp))
    partial_force = jnp.sum(inertia * new_disp, axis=1)
    force = sum_all(partial_force, "plate") * (8.0 / math.sqrt(total_cols * total_rows))
    every_force = gather_all(force, "storey").reshape(-1)
    every_shear = jnp.cumsum(every_force[::-1])[::-1]
    every_drift = jnp.cumsum(every_shear) / total_rows
    here_storey = lax.axis_index("storey")
    shear = lax.dynamic_slice_in_dim(every_shear, here_storey * rows, rows)
    drift = lax.dynamic_slice_in_dim(every_drift, here_storey * rows, rows)
    target = inertia * drift[:, None]
    adjoint = jnp.zeros_like(load)
    resid = target
    for step in range(ITERS):
        adjoint = adjoint + correct(resid, True)
        if step < ITERS - 1:
            resid = target - (diag * adjoint - neighbours(stiff * adjoint))
    partial_sums = damper_totals(damper_map, adjoint * new_disp, damper_coef.shape[0])
    sums = sum_all(partial_sums, "plate")
    grads = -CD * 64.0 / math.sqrt(rows * total_cols / damper_coef.shape[0]) * sums
    return (new_disp, adjoint, shear, grads)


def solution(mesh):
    return jax.shard_map(
        on_device,
        mesh=mesh,
        in_specs=(
            P("storey", "plate"),
            P("storey", "plate"),
            P("storey", "plate"),
            P("storey", "plate"),
            P(),
            P("storey", "plate"),
            P("storey"),
            P("storey", "plate"),
            P("storey", "plate"),
            P("storey"),
            P("storey", "plate"),
        ),
        out_specs=(P("storey", "plate"), P("storey", "plate"), P("storey"), P("storey")),
        check_vma=False,
    )
```

```python
import math

import jax
import jax.numpy as jnp
from jax import lax
from jax.sharding import PartitionSpec as P

ITERS = 6


KF = 5.0 / 9.0
CM = 2.16
CD = 1.1
HIGH = lax.Precision.HIGHEST


def shifted(x, axis, dim, toward):
    devices, length = (lax.axis_size(axis), x.shape[dim])
    if toward > 0:
        pairs = [(i, i + 1) for i in range(devices - 1)]
        edge = lax.slice_in_dim(x, length - 1, length, axis=dim)
    else:
        pairs = [(i + 1, i) for i in range(devices - 1)]
        edge = lax.slice_in_dim(x, 0, 1, axis=dim)
    return lax.ppermute(edge, axis, pairs)


def gather_all(value, axis):
    devices = lax.axis_size(axis)
    spread = jnp.broadcast_to(value[None], (devices,) + value.shape)
    return lax.all_to_all(spread, axis, 0, 0, tiled=False)


def sum_all(value, axis):
    return jnp.sum(gather_all(value, axis), axis=0)


def halos(field):
    above = shifted(field, "storey", 0, 1)
    below = shifted(field, "storey", 0, -1)
    left = shifted(field, "plate", 1, 1)
    right = shifted(field, "plate", 1, -1)
    return above, below, left, right


def around(field, above, below, left, right):
    vertical = jnp.concatenate([above, field[:-1]], axis=0) + jnp.concatenate([field[1:], below], axis=0)
    horizontal = jnp.concatenate([left, field[:, :-1]], axis=1) + jnp.concatenate([field[:, 1:], right], axis=1)
    return vertical + horizontal


def around_nodes(field, sides, places):
    above, below, left, right = sides
    rows, cols = field.shape
    node_row = places // cols
    node_col = places % cols
    spots = jnp.stack([places - cols, places + cols, places - 1, places + 1])
    near = field.reshape(-1)[jnp.clip(spots, 0, rows * cols - 1)]
    rim = jnp.concatenate([above[0], below[0], left[:, 0], right[:, 0]])
    rim_at = jnp.stack([node_col, cols + node_col, 2 * cols + node_row, 2 * cols + rows + node_row])
    far = rim[rim_at]
    up = jnp.where(node_row > 0, near[0], far[0])
    down = jnp.where(node_row < rows - 1, near[1], far[1])
    west = jnp.where(node_col > 0, near[2], far[2])
    east = jnp.where(node_col < cols - 1, near[3], far[3])
    return (up + down) + (west + east)


def damper_lookup(ids, coef):
    labels = jnp.arange(coef.shape[0], dtype=jnp.int32)
    match = ids[None, :, :] == labels[:, None, None]
    return jnp.sum(jnp.where(match, coef[:, None, None], 0.0), axis=0)


def damper_totals(ids, values, count):
    labels = jnp.arange(count, dtype=jnp.int32)
    match = ids[None, :, :] == labels[:, None, None]
    return jnp.sum(jnp.where(match, values[None, :, :], 0.0), axis=(1, 2))


def panel_slabs(panel_store, owner, nodes):
    n_plate = lax.axis_size("plate")
    mine = lax.axis_index("plate") == owner
    rows_of = panel_store.reshape(n_plate, nodes, -1)
    cols_of = jnp.swapaxes(panel_store.reshape(-1, n_plate, nodes), 0, 1)
    cols_of = jnp.swapaxes(cols_of, 1, 2)

    both = jnp.concatenate([rows_of, cols_of], axis=1)
    sent = jnp.where(mine, both, 0.0)
    got = jnp.sum(lax.all_to_all(sent, "plate", 0, 0, tiled=False), axis=0)
    return got[:nodes], got[nodes:]


def on_device(
    load,
    disp,
    mass,
    wall_class,
    class_stiff,
    damper_map,
    damper_coef,
    band_tile,
    panel_store,
    owner,
    node_index,
):
    rows, cols = load.shape
    n_storey = lax.axis_size("storey")
    n_plate = lax.axis_size("plate")
    total_rows = rows * n_storey
    total_cols = cols * n_plate
    nodes = node_index.shape[1]
    stiff = jnp.zeros_like(load)
    for level in range(class_stiff.shape[0]):
        stiff = stiff + jnp.where(wall_class == level, class_stiff[level], 0.0)
    stiff = KF * stiff
    inertia = CM * mass
    damping = CD * damper_lookup(damper_map, damper_coef)
    diag = 4.0 * stiff + inertia + damping
    places = node_index[0]
    row_slab, col_slab = panel_slabs(panel_store, owner[0], nodes)

    def correct(resid, picked, transpose, first=False):
        scaled = resid / diag
        if transpose:
            result = lax.dot_general(scaled, band_tile, (((1,), (1,)), ((), ())), precision=HIGH)
        else:
            result = jnp.dot(scaled, band_tile, precision=HIGH)
        if first:
            picked = picked + 0.0 * row_slab[0, 0]
        values = gather_all(picked, "plate").reshape(-1)
        slab = col_slab if transpose else row_slab
        mine = jnp.dot(slab, values, precision=HIGH)
        return result.reshape(-1).at[places].add(mine).reshape(rows, cols)

    def at(field):
        return field.reshape(-1)[places]

    load_n, diag_n, stiff_n = at(load), at(diag), at(stiff)
    new_disp = disp
    for step in range(ITERS):
        sides = halos(new_disp)
        resid = load - (diag * new_disp - stiff * around(new_disp, *sides))
        picked = load_n - (diag_n * at(new_disp) - stiff_n * around_nodes(new_disp, sides, places))
        new_disp = new_disp + correct(resid, picked, False, first=step == 0)
    partial_force = jnp.sum(inertia * new_disp, axis=1)
    force = sum_all(partial_force, "plate") * (8.0 / math.sqrt(total_cols * total_rows))
    every_force = gather_all(force, "storey").reshape(-1)
    every_shear = jnp.cumsum(every_force[::-1])[::-1]
    every_drift = jnp.cumsum(every_shear) / total_rows
    here_storey = lax.axis_index("storey")
    shear = lax.dynamic_slice_in_dim(every_shear, here_storey * rows, rows)
    drift = lax.dynamic_slice_in_dim(every_drift, here_storey * rows, rows)
    target = inertia * drift[:, None]
    adjoint = jnp.zeros_like(load)
    target_n = at(target)
    resid = target
    picked = target_n
    for step in range(ITERS):
        adjoint = adjoint + correct(resid, picked, True)
        if step < ITERS - 1:
            spread = stiff * adjoint
            sides = halos(spread)
            resid = target - (diag * adjoint - around(spread, *sides))
            picked = target_n - (diag_n * at(adjoint) - around_nodes(spread, sides, places))
    partial_sums = damper_totals(damper_map, adjoint * new_disp, damper_coef.shape[0])
    sums = sum_all(partial_sums, "plate")
    grads = -CD * 64.0 / math.sqrt(rows * total_cols / damper_coef.shape[0]) * sums
    return (new_disp, adjoint, shear, grads)


def solution(mesh):
    return jax.shard_map(
        on_device,
        mesh=mesh,
        in_specs=(
            P("storey", "plate"),
            P("storey", "plate"),
            P("storey", "plate"),
            P("storey", "plate"),
            P(),
            P("storey", "plate"),
            P("storey"),
            P("storey", "plate"),
            P("storey", "plate"),
            P("storey"),
            P("storey", "plate"),
        ),
        out_specs=(P("storey", "plate"), P("storey", "plate"), P("storey"), P("storey")),
        check_vma=False,
    )
```

```python
import math

import jax
import jax.numpy as jnp
from jax import lax
from jax.sharding import PartitionSpec as P

ITERS = 6


KF = 5.0 / 9.0
CM = 2.16
CD = 1.1
HIGH = lax.Precision.HIGHEST


def shifted(x, axis, dim, toward):
    devices, length = (lax.axis_size(axis), x.shape[dim])
    if toward > 0:
        pairs = [(i, i + 1) for i in range(devices - 1)]
        edge = lax.slice_in_dim(x, length - 1, length, axis=dim)
    else:
        pairs = [(i + 1, i) for i in range(devices - 1)]
        edge = lax.slice_in_dim(x, 0, 1, axis=dim)
    return lax.ppermute(edge, axis, pairs)


def gather_all(value, axis):
    devices = lax.axis_size(axis)
    spread = jnp.broadcast_to(value[None], (devices,) + value.shape)
    return lax.all_to_all(spread, axis, 0, 0, tiled=False)


def sum_all(value, axis):
    return jnp.sum(gather_all(value, axis), axis=0)


def neighbours(field):
    above = shifted(field, "storey", 0, 1)
    below = shifted(field, "storey", 0, -1)
    left = shifted(field, "plate", 1, 1)
    right = shifted(field, "plate", 1, -1)
    vertical = jnp.concatenate([above, field[:-1]], axis=0) + jnp.concatenate([field[1:], below], axis=0)
    horizontal = jnp.concatenate([left, field[:, :-1]], axis=1) + jnp.concatenate([field[:, 1:], right], axis=1)
    return vertical + horizontal


def damper_lookup(ids, coef):
    labels = jnp.arange(coef.shape[0], dtype=jnp.int32)
    match = ids[None, :, :] == labels[:, None, None]
    return jnp.sum(jnp.where(match, coef[:, None, None], 0.0), axis=0)


def damper_totals(ids, values, count):
    labels = jnp.arange(count, dtype=jnp.int32)
    match = ids[None, :, :] == labels[:, None, None]
    return jnp.sum(jnp.where(match, values[None, :, :], 0.0), axis=(1, 2))


def panel_slabs(panel_store, owner, nodes):
    n_plate = lax.axis_size("plate")
    rows_of = panel_store.reshape(n_plate, nodes, -1)
    got_rows = lax.all_to_all(rows_of, "plate", 0, 0, tiled=False)
    cols_of = panel_store.reshape(-1, n_plate, nodes)
    got_cols = lax.all_to_all(cols_of, "plate", 1, 1, tiled=False)
    row_slab = lax.dynamic_index_in_dim(got_rows, owner, 0, keepdims=False)
    col_slab = lax.dynamic_index_in_dim(got_cols, owner, 1, keepdims=False).T
    return row_slab, col_slab


def on_device(
    load,
    disp,
    mass,
    wall_class,
    class_stiff,
    damper_map,
    damper_coef,
    band_tile,
    panel_store,
    owner,
    node_index,
):
    rows, cols = load.shape
    n_storey = lax.axis_size("storey")
    n_plate = lax.axis_size("plate")
    total_rows = rows * n_storey
    total_cols = cols * n_plate
    nodes = node_index.shape[1]
    stiff = jnp.zeros_like(load)
    for level in range(class_stiff.shape[0]):
        stiff = stiff + jnp.where(wall_class == level, class_stiff[level], 0.0)
    stiff = KF * stiff
    inertia = CM * mass
    damping = CD * damper_lookup(damper_map, damper_coef)
    diag = 4.0 * stiff + inertia + damping
    places = node_index[0]
    row_slab, col_slab = panel_slabs(panel_store, owner[0], nodes)

    def correct(resid, transpose, first=False):
        scaled = resid / diag
        if transpose:
            result = lax.dot_general(scaled, band_tile, (((1,), (1,)), ((), ())), precision=HIGH)
        else:
            result = jnp.dot(scaled, band_tile, precision=HIGH)
        picked = resid.reshape(-1)[places]
        if first:
            picked = picked + 0.0 * row_slab[0, 0]
        values = gather_all(picked, "plate").reshape(-1)
        slab = col_slab if transpose else row_slab
        mine = jnp.dot(slab, values, precision=HIGH)
        return result.reshape(-1).at[places].add(mine).reshape(rows, cols)

    new_disp = disp
    resid = load - (diag * new_disp - stiff * neighbours(new_disp))
    for step in range(ITERS):
        new_disp = new_disp + correct(resid, False, first=step == 0)
        if step < ITERS - 1:
            resid = load - (diag * new_disp - stiff * neighbours(new_disp))
    partial_force = jnp.sum(inertia * new_disp, axis=1)
    force = sum_all(partial_force, "plate") * (8.0 / math.sqrt(total_cols * total_rows))
    every_force = gather_all(force, "storey").reshape(-1)
    every_shear = jnp.cumsum(every_force[::-1])[::-1]
    every_drift = jnp.cumsum(every_shear) / total_rows
    here_storey = lax.axis_index("storey")
    shear = lax.dynamic_slice_in_dim(every_shear, here_storey * rows, rows)
    drift = lax.dynamic_slice_in_dim(every_drift, here_storey * rows, rows)
    target = inertia * drift[:, None]
    adjoint = jnp.zeros_like(load)
    resid = target
    for step in range(ITERS):
        adjoint = adjoint + correct(resid, True)
        if step < ITERS - 1:
            resid = target - (diag * adjoint - neighbours(stiff * adjoint))
    partial_sums = damper_totals(damper_map, adjoint * new_disp, damper_coef.shape[0])
    sums = sum_all(partial_sums, "plate")
    grads = -CD * 64.0 / math.sqrt(rows * total_cols / damper_coef.shape[0]) * sums
    return (new_disp, adjoint, shear, grads)


def solution(mesh):
    return jax.shard_map(
        on_device,
        mesh=mesh,
        in_specs=(
            P("storey", "plate"),
            P("storey", "plate"),
            P("storey", "plate"),
            P("storey", "plate"),
            P(),
            P("storey", "plate"),
            P("storey"),
            P("storey", "plate"),
            P("storey", "plate"),
            P("storey"),
            P("storey", "plate"),
        ),
        out_specs=(P("storey", "plate"), P("storey", "plate"), P("storey"), P("storey")),
        check_vma=False,
    )
```

```python
import math

import jax
import jax.numpy as jnp
from jax import lax
from jax.sharding import PartitionSpec as P

ITERS = 6


KF = 5.0 / 9.0
CM = 2.16
CD = 1.1
HIGH = lax.Precision.HIGHEST


def shifted(x, axis, dim, toward):
    devices, length = (lax.axis_size(axis), x.shape[dim])
    if toward > 0:
        pairs = [(i, i + 1) for i in range(devices - 1)]
        edge = lax.slice_in_dim(x, length - 1, length, axis=dim)
    else:
        pairs = [(i + 1, i) for i in range(devices - 1)]
        edge = lax.slice_in_dim(x, 0, 1, axis=dim)
    return lax.ppermute(edge, axis, pairs)


def gather_all(value, axis):
    devices = lax.axis_size(axis)
    spread = jnp.broadcast_to(value[None], (devices,) + value.shape)
    return lax.all_to_all(spread, axis, 0, 0, tiled=False)


def sum_all(value, axis):
    return jnp.sum(gather_all(value, axis), axis=0)


def neighbours(field):
    above = shifted(field, "storey", 0, 1)
    below = shifted(field, "storey", 0, -1)
    left = shifted(field, "plate", 1, 1)
    right = shifted(field, "plate", 1, -1)
    vertical = jnp.concatenate([above, field[:-1]], axis=0) + jnp.concatenate([field[1:], below], axis=0)
    horizontal = jnp.concatenate([left, field[:, :-1]], axis=1) + jnp.concatenate([field[:, 1:], right], axis=1)
    return vertical + horizontal


def damper_lookup(ids, coef):
    labels = jnp.arange(coef.shape[0], dtype=jnp.int32)
    match = ids[None, :, :] == labels[:, None, None]
    return jnp.sum(jnp.where(match, coef[:, None, None], 0.0), axis=0)


def damper_totals(ids, values, count):
    labels = jnp.arange(count, dtype=jnp.int32)
    match = ids[None, :, :] == labels[:, None, None]
    return jnp.sum(jnp.where(match, values[None, :, :], 0.0), axis=(1, 2))


def panel_slabs(panel_store, owner, nodes, weights, node_rows):
    n_plate = lax.axis_size("plate")
    here = lax.axis_index("plate")
    mine = here == owner
    rows_of = panel_store.reshape(n_plate, nodes, -1)
    cols_of = jnp.swapaxes(panel_store.reshape(-1, n_plate, nodes), 0, 1)
    cols_of = jnp.swapaxes(cols_of, 1, 2)
    spots = jnp.arange(n_plate * nodes, dtype=jnp.int32) // nodes == here
    info = jnp.stack([jnp.where(spots, jnp.tile(weights, n_plate), 0.0), jnp.where(spots, jnp.tile(node_rows, n_plate), 0.0)])
    both = jnp.concatenate([jnp.where(mine, jnp.concatenate([rows_of, cols_of], axis=1), 0.0), jnp.broadcast_to(info[None], (n_plate,) + info.shape)], axis=1)
    got = jnp.sum(lax.all_to_all(both, "plate", 0, 0, tiled=False), axis=0)
    return got[:nodes], got[nodes:2 * nodes], got[2 * nodes], got[2 * nodes + 1]


def on_device(
    load,
    disp,
    mass,
    wall_class,
    class_stiff,
    damper_map,
    damper_coef,
    band_tile,
    panel_store,
    owner,
    node_index,
):
    rows, cols = load.shape
    n_storey = lax.axis_size("storey")
    n_plate = lax.axis_size("plate")
    total_rows = rows * n_storey
    total_cols = cols * n_plate
    nodes = node_index.shape[1]
    stiff = jnp.zeros_like(load)
    for level in range(class_stiff.shape[0]):
        stiff = stiff + jnp.where(wall_class == level, class_stiff[level], 0.0)
    stiff = KF * stiff
    inertia = CM * mass
    damping = CD * damper_lookup(damper_map, damper_coef)
    diag = 4.0 * stiff + inertia + damping
    places = node_index[0]
    node_rows = (places // cols).astype(jnp.float32)
    row_slab, col_slab, group_weights, group_rows = panel_slabs(panel_store, owner[0], nodes, inertia.reshape(-1)[places], node_rows)
    group_rows = group_rows.astype(jnp.int32)

    def correct(resid, transpose, first=False, values=None):
        scaled = resid / diag
        if transpose:
            result = lax.dot_general(scaled, band_tile, (((1,), (1,)), ((), ())), precision=HIGH)
        else:
            result = jnp.dot(scaled, band_tile, precision=HIGH)
        if values is None:
            picked = resid.reshape(-1)[places]
            if first:
                picked = picked + 0.0 * row_slab[0, 0]
            values = gather_all(picked, "plate").reshape(-1)
        slab = col_slab if transpose else row_slab
        mine = jnp.dot(slab, values, precision=HIGH)
        return result.reshape(-1).at[places].add(mine).reshape(rows, cols)

    new_disp = disp
    resid = load - (diag * new_disp - stiff * neighbours(new_disp))
    for step in range(ITERS):
        new_disp = new_disp + correct(resid, False, first=step == 0)
        if step < ITERS - 1:
            resid = load - (diag * new_disp - stiff * neighbours(new_disp))
    partial_force = jnp.sum(inertia * new_disp, axis=1) * (8.0 / math.sqrt(total_cols * total_rows))
    column_force = gather_all(partial_force, "storey").reshape(-1)
    column_shear = jnp.cumsum(column_force[::-1])[::-1]
    column_drift = jnp.cumsum(column_shear) / total_rows
    here_storey = lax.axis_index("storey")
    part_shear = lax.dynamic_slice_in_dim(column_shear, here_storey * rows, rows)
    part_drift = lax.dynamic_slice_in_dim(column_drift, here_storey * rows, rows)
    totals = sum_all(jnp.concatenate([part_shear, part_drift]), "plate")
    shear = totals[:rows]
    drift = totals[rows:]
    target = inertia * drift[:, None]
    first_values = group_weights * drift[group_rows]
    adjoint = jnp.zeros_like(load)
    resid = target
    for step in range(ITERS):
        adjoint = adjoint + correct(resid, True, values=first_values if step == 0 else None)
        if step < ITERS - 1:
            resid = target - (diag * adjoint - neighbours(stiff * adjoint))
    partial_sums = damper_totals(damper_map, adjoint * new_disp, damper_coef.shape[0])
    sums = sum_all(partial_sums, "plate")
    grads = -CD * 64.0 / math.sqrt(rows * total_cols / damper_coef.shape[0]) * sums
    return (new_disp, adjoint, shear, grads)


def solution(mesh):
    return jax.shard_map(
        on_device,
        mesh=mesh,
        in_specs=(
            P("storey", "plate"),
            P("storey", "plate"),
            P("storey", "plate"),
            P("storey", "plate"),
            P(),
            P("storey", "plate"),
            P("storey"),
            P("storey", "plate"),
            P("storey", "plate"),
            P("storey"),
            P("storey", "plate"),
        ),
        out_specs=(P("storey", "plate"), P("storey", "plate"), P("storey"), P("storey")),
        check_vma=False,
    )
```

```python
import math

import jax
import jax.numpy as jnp
from jax import lax
from jax.sharding import PartitionSpec as P

ITERS = 6


KF = 5.0 / 9.0
CM = 2.16
CD = 1.1
HIGH = lax.Precision.HIGHEST


def shifted(x, axis, dim, toward):
    devices, length = (lax.axis_size(axis), x.shape[dim])
    if toward > 0:
        pairs = [(i, i + 1) for i in range(devices - 1)]
        edge = lax.slice_in_dim(x, length - 1, length, axis=dim)
    else:
        pairs = [(i + 1, i) for i in range(devices - 1)]
        edge = lax.slice_in_dim(x, 0, 1, axis=dim)
    return lax.ppermute(edge, axis, pairs)


def gather_all(value, axis):
    devices = lax.axis_size(axis)
    spread = jnp.broadcast_to(value[None], (devices,) + value.shape)
    return lax.all_to_all(spread, axis, 0, 0, tiled=False)


def sum_all(value, axis):
    return jnp.sum(gather_all(value, axis), axis=0)


def neighbours(field):
    above = shifted(field, "storey", 0, 1)
    below = shifted(field, "storey", 0, -1)
    left = shifted(field, "plate", 1, 1)
    right = shifted(field, "plate", 1, -1)
    vertical = jnp.concatenate([above, field[:-1]], axis=0) + jnp.concatenate([field[1:], below], axis=0)
    horizontal = jnp.concatenate([left, field[:, :-1]], axis=1) + jnp.concatenate([field[:, 1:], right], axis=1)
    return vertical + horizontal


def damper_lookup(ids, coef):
    labels = jnp.arange(coef.shape[0], dtype=jnp.int32)
    match = ids[None, :, :] == labels[:, None, None]
    return jnp.sum(jnp.where(match, coef[:, None, None], 0.0), axis=0)


def damper_totals(ids, values, count):
    labels = jnp.arange(count, dtype=jnp.int32)
    match = ids[None, :, :] == labels[:, None, None]
    return jnp.sum(jnp.where(match, values[None, :, :], 0.0), axis=(1, 2))


def panel_slabs(panel_store, owner, nodes):
    n_plate = lax.axis_size("plate")
    mine = lax.axis_index("plate") == owner
    rows_of = panel_store.reshape(n_plate, nodes, -1)
    cols_of = jnp.swapaxes(panel_store.reshape(-1, n_plate, nodes), 0, 1)
    cols_of = jnp.swapaxes(cols_of, 1, 2)

    both = jnp.concatenate([rows_of, cols_of], axis=1)
    sent = jnp.where(mine, both, 0.0)
    got = jnp.sum(lax.all_to_all(sent, "plate", 0, 0, tiled=False), axis=0)
    return got[:nodes], got[nodes:]


def on_device(
    load,
    disp,
    mass,
    wall_class,
    class_stiff,
    damper_map,
    damper_coef,
    band_tile,
    panel_store,
    owner,
    node_index,
):
    rows, cols = load.shape
    n_storey = lax.axis_size("storey")
    n_plate = lax.axis_size("plate")
    total_rows = rows * n_storey
    total_cols = cols * n_plate
    nodes = node_index.shape[1]
    stiff = jnp.zeros_like(load)
    for level in range(class_stiff.shape[0]):
        stiff = stiff + jnp.where(wall_class == level, class_stiff[level], 0.0)
    stiff = KF * stiff
    inertia = CM * mass
    damping = CD * damper_lookup(damper_map, damper_coef)
    diag = 4.0 * stiff + inertia + damping
    places = node_index[0]
    node_rows = (places // cols).astype(jnp.float32)
    row_slab, col_slab = panel_slabs(panel_store, owner[0], nodes)
    node_info = jnp.concatenate([inertia.reshape(-1)[places], node_rows])
    group_info = {}

    def correct(resid, transpose, first=False, values=None):
        scaled = resid / diag
        if transpose:
            result = lax.dot_general(scaled, band_tile, (((1,), (1,)), ((), ())), precision=HIGH)
        else:
            result = jnp.dot(scaled, band_tile, precision=HIGH)
        if values is None:
            picked = resid.reshape(-1)[places]
            if first:
                picked = jnp.concatenate([picked + 0.0 * row_slab[0, 0], node_info])
            got = gather_all(picked, "plate")
            if first:
                group_info["weights"] = got[:, nodes:2 * nodes].reshape(-1)
                group_info["rows"] = got[:, 2 * nodes:].reshape(-1).astype(jnp.int32)
            values = got[:, :nodes].reshape(-1)
        slab = col_slab if transpose else row_slab
        mine = jnp.dot(slab, values, precision=HIGH)
        return result.reshape(-1).at[places].add(mine).reshape(rows, cols)

    new_disp = disp
    resid = load - (diag * new_disp - stiff * neighbours(new_disp))
    for step in range(ITERS):
        new_disp = new_disp + correct(resid, False, first=step == 0)
        if step < ITERS - 1:
            resid = load - (diag * new_disp - stiff * neighbours(new_disp))
    partial_force = jnp.sum(inertia * new_disp, axis=1) * (8.0 / math.sqrt(total_cols * total_rows))
    column_force = gather_all(partial_force, "storey").reshape(-1)
    column_shear = jnp.cumsum(column_force[::-1])[::-1]
    column_drift = jnp.cumsum(column_shear) / total_rows
    here_storey = lax.axis_index("storey")
    part_shear = lax.dynamic_slice_in_dim(column_shear, here_storey * rows, rows)
    part_drift = lax.dynamic_slice_in_dim(column_drift, here_storey * rows, rows)
    totals = sum_all(jnp.concatenate([part_shear, part_drift]), "plate")
    shear = totals[:rows]
    drift = totals[rows:]
    target = inertia * drift[:, None]
    first_values = group_info["weights"] * drift[group_info["rows"]]
    adjoint = jnp.zeros_like(load)
    resid = target
    for step in range(ITERS):
        adjoint = adjoint + correct(resid, True, values=first_values if step == 0 else None)
        if step < ITERS - 1:
            resid = target - (diag * adjoint - neighbours(stiff * adjoint))
    partial_sums = damper_totals(damper_map, adjoint * new_disp, damper_coef.shape[0])
    sums = sum_all(partial_sums, "plate")
    grads = -CD * 64.0 / math.sqrt(rows * total_cols / damper_coef.shape[0]) * sums
    return (new_disp, adjoint, shear, grads)


def solution(mesh):
    return jax.shard_map(
        on_device,
        mesh=mesh,
        in_specs=(
            P("storey", "plate"),
            P("storey", "plate"),
            P("storey", "plate"),
            P("storey", "plate"),
            P(),
            P("storey", "plate"),
            P("storey"),
            P("storey", "plate"),
            P("storey", "plate"),
            P("storey"),
            P("storey", "plate"),
        ),
        out_specs=(P("storey", "plate"), P("storey", "plate"), P("storey"), P("storey")),
        check_vma=False,
    )
```

```python
import math

import jax
import jax.numpy as jnp
from jax import lax
from jax.sharding import PartitionSpec as P

ITERS = 6


KF = 5.0 / 9.0
CM = 2.16
CD = 1.1
HIGH = lax.Precision.HIGHEST


def shifted(x, axis, dim, toward):
    devices, length = (lax.axis_size(axis), x.shape[dim])
    position = lax.axis_index(axis)
    if toward > 0:
        pairs = [(i, (i + 1) % devices) for i in range(devices)]
        edge = lax.slice_in_dim(x, length - 1, length, axis=dim)
        outside = position == 0
    else:
        pairs = [((i + 1) % devices, i) for i in range(devices)]
        edge = lax.slice_in_dim(x, 0, 1, axis=dim)
        outside = position == devices - 1
    return jnp.where(outside, 0.0, lax.ppermute(edge, axis, pairs))


def gather_all(value, axis):
    devices = lax.axis_size(axis)
    spread = jnp.broadcast_to(value[None], (devices,) + value.shape)
    return lax.all_to_all(spread, axis, 0, 0, tiled=False)


def sum_all(value, axis):
    return jnp.sum(gather_all(value, axis), axis=0)


def neighbours(field):
    above = shifted(field, "storey", 0, 1)
    below = shifted(field, "storey", 0, -1)
    left = shifted(field, "plate", 1, 1)
    right = shifted(field, "plate", 1, -1)
    vertical = jnp.concatenate([above, field[:-1]], axis=0) + jnp.concatenate([field[1:], below], axis=0)
    horizontal = jnp.concatenate([left, field[:, :-1]], axis=1) + jnp.concatenate([field[:, 1:], right], axis=1)
    return vertical + horizontal


def damper_lookup(ids, coef):
    labels = jnp.arange(coef.shape[0], dtype=jnp.int32)
    match = ids[None, :, :] == labels[:, None, None]
    return jnp.sum(jnp.where(match, coef[:, None, None], 0.0), axis=0)


def damper_totals(ids, values, count):
    labels = jnp.arange(count, dtype=jnp.int32)
    match = ids[None, :, :] == labels[:, None, None]
    return jnp.sum(jnp.where(match, values[None, :, :], 0.0), axis=(1, 2))


def panel_slabs(panel_store, owner, nodes):
    n_plate = lax.axis_size("plate")
    mine = lax.axis_index("plate") == owner
    rows_of = panel_store.reshape(n_plate, nodes, -1)
    cols_of = jnp.swapaxes(panel_store.reshape(-1, n_plate, nodes), 0, 1)
    cols_of = jnp.swapaxes(cols_of, 1, 2)

    both = jnp.concatenate([rows_of, cols_of], axis=1)
    sent = jnp.where(mine, both, 0.0)
    got = jnp.sum(lax.all_to_all(sent, "plate", 0, 0, tiled=False), axis=0)
    return got[:nodes], got[nodes:]


def on_device(
    load,
    disp,
    mass,
    wall_class,
    class_stiff,
    damper_map,
    damper_coef,
    band_tile,
    panel_store,
    owner,
    node_index,
):
    rows, cols = load.shape
    n_storey = lax.axis_size("storey")
    n_plate = lax.axis_size("plate")
    total_rows = rows * n_storey
    total_cols = cols * n_plate
    nodes = node_index.shape[1]
    stiff = jnp.zeros_like(load)
    for level in range(class_stiff.shape[0]):
        stiff = stiff + jnp.where(wall_class == level, class_stiff[level], 0.0)
    stiff = KF * stiff
    inertia = CM * mass
    damping = CD * damper_lookup(damper_map, damper_coef)
    diag = 4.0 * stiff + inertia + damping
    places = node_index[0]
    row_slab, col_slab = panel_slabs(panel_store, owner[0], nodes)

    def correct(resid, transpose, first=False):
        scaled = resid / diag
        if transpose:
            result = lax.dot_general(scaled, band_tile, (((1,), (1,)), ((), ())), precision=HIGH)
        else:
            result = jnp.dot(scaled, band_tile, precision=HIGH)
        picked = resid.reshape(-1)[places]
        if first:
            picked = picked + 0.0 * row_slab[0, 0]
        values = gather_all(picked, "plate").reshape(-1)
        slab = col_slab if transpose else row_slab
        mine = jnp.dot(slab, values, precision=HIGH)
        return result.reshape(-1).at[places].add(mine).reshape(rows, cols)

    new_disp = disp
    resid = load - (diag * new_disp - stiff * neighbours(new_disp))
    for step in range(ITERS):
        new_disp = new_disp + correct(resid, False, first=step == 0)
        if step < ITERS - 1:
            resid = load - (diag * new_disp - stiff * neighbours(new_disp))
    partial_force = jnp.sum(inertia * new_disp, axis=1)
    force = sum_all(partial_force, "plate") * (8.0 / math.sqrt(total_cols * total_rows))
    every_force = gather_all(force, "storey").reshape(-1)
    every_shear = jnp.cumsum(every_force[::-1])[::-1]
    every_drift = jnp.cumsum(every_shear) / total_rows
    here_storey = lax.axis_index("storey")
    shear = lax.dynamic_slice_in_dim(every_shear, here_storey * rows, rows)
    drift = lax.dynamic_slice_in_dim(every_drift, here_storey * rows, rows)
    target = inertia * drift[:, None]
    adjoint = jnp.zeros_like(load)
    resid = target
    for step in range(ITERS):
        adjoint = adjoint + correct(resid, True)
        if step < ITERS - 1:
            resid = target - (diag * adjoint - neighbours(stiff * adjoint))
    partial_sums = damper_totals(damper_map, adjoint * new_disp, damper_coef.shape[0])
    sums = sum_all(partial_sums, "plate")
    grads = -CD * 64.0 / math.sqrt(rows * total_cols / damper_coef.shape[0]) * sums
    return (new_disp, adjoint, shear, grads)


def solution(mesh):
    return jax.shard_map(
        on_device,
        mesh=mesh,
        in_specs=(
            P("storey", "plate"),
            P("storey", "plate"),
            P("storey", "plate"),
            P("storey", "plate"),
            P(),
            P("storey", "plate"),
            P("storey"),
            P("storey", "plate"),
            P("storey", "plate"),
            P("storey"),
            P("storey", "plate"),
        ),
        out_specs=(P("storey", "plate"), P("storey", "plate"), P("storey"), P("storey")),
        check_vma=False,
    )
```

```python
import math

import jax
import jax.numpy as jnp
from jax import lax
from jax.sharding import PartitionSpec as P

ITERS = 6


KF = 5.0 / 9.0
CM = 2.16
CD = 1.1
HIGH = lax.Precision.HIGHEST


def shifted(x, axis, dim, toward):
    devices, length = (lax.axis_size(axis), x.shape[dim])
    if toward > 0:
        pairs = [(i, i + 1) for i in range(devices - 1)]
        edge = lax.slice_in_dim(x, length - 1, length, axis=dim)
    else:
        pairs = [(i + 1, i) for i in range(devices - 1)]
        edge = lax.slice_in_dim(x, 0, 1, axis=dim)
    return lax.ppermute(edge, axis, pairs)


def gather_all(value, axis):
    devices = lax.axis_size(axis)
    spread = jnp.broadcast_to(value[None], (devices,) + value.shape)
    return lax.all_to_all(spread, axis, 0, 0, tiled=False)


def sum_all(value, axis):
    return jnp.sum(gather_all(value, axis), axis=0)


def neighbours(field):
    above = shifted(field, "storey", 0, 1)
    below = shifted(field, "storey", 0, -1)
    left = shifted(field, "plate", 1, 1)
    right = shifted(field, "plate", 1, -1)
    vertical = jnp.concatenate([above, field[:-1]], axis=0) + jnp.concatenate([field[1:], below], axis=0)
    horizontal = jnp.concatenate([left, field[:, :-1]], axis=1) + jnp.concatenate([field[:, 1:], right], axis=1)
    return vertical + horizontal


def damper_lookup(ids, coef):
    labels = jnp.arange(coef.shape[0], dtype=jnp.int32)
    match = ids[None, :, :] == labels[:, None, None]
    return jnp.sum(jnp.where(match, coef[:, None, None], 0.0), axis=0)


def damper_totals(ids, values, count):
    labels = jnp.arange(count, dtype=jnp.int32)
    match = ids[None, :, :] == labels[:, None, None]
    return jnp.sum(jnp.where(match, values[None, :, :], 0.0), axis=(1, 2))


def panel_slabs(panel_store, owner, nodes):
    n_plate = lax.axis_size("plate")
    mine = lax.axis_index("plate") == owner
    rows_of = panel_store.reshape(n_plate, nodes, -1)
    cols_of = jnp.swapaxes(panel_store.reshape(-1, n_plate, nodes), 0, 1)
    cols_of = jnp.swapaxes(cols_of, 1, 2)

    both = jnp.concatenate([rows_of, cols_of], axis=1)
    sent = jnp.where(mine, both, 0.0)
    got = jnp.sum(lax.all_to_all(sent, "plate", 0, 0, tiled=False), axis=0)
    return got[:nodes], got[nodes:]


def on_device(
    load,
    disp,
    mass,
    wall_class,
    class_stiff,
    damper_map,
    damper_coef,
    band_tile,
    panel_store,
    owner,
    node_index,
):
    rows, cols = load.shape
    n_storey = lax.axis_size("storey")
    n_plate = lax.axis_size("plate")
    total_rows = rows * n_storey
    total_cols = cols * n_plate
    nodes = node_index.shape[1]
    stiff = jnp.zeros_like(load)
    for level in range(class_stiff.shape[0]):
        stiff = stiff + jnp.where(wall_class == level, class_stiff[level], 0.0)
    stiff = KF * stiff
    inertia = CM * mass
    damping = CD * damper_lookup(damper_map, damper_coef)
    diag = 4.0 * stiff + inertia + damping
    places = node_index[0]
    row_slab, col_slab = panel_slabs(panel_store, owner[0], nodes)

    def correct(resid, transpose, first=False):
        scaled = resid / diag
        if transpose:
            result = lax.dot_general(scaled, band_tile, (((1,), (1,)), ((), ())), precision=HIGH)
        else:
            result = jnp.dot(scaled, band_tile, precision=HIGH)
        picked = resid.reshape(-1)[places]
        if first:
            picked = picked + 0.0 * row_slab[0, 0]
        values = gather_all(picked, "plate").reshape(-1)
        slab = col_slab if transpose else row_slab
        mine = jnp.dot(slab, values, precision=HIGH)
        return result.reshape(-1).at[places].add(mine).reshape(rows, cols)

    new_disp = disp
    resid = load - (diag * new_disp - stiff * neighbours(new_disp))
    for step in range(ITERS):
        new_disp = new_disp + correct(resid, False, first=step == 0)
        if step < ITERS - 1:
            resid = load - (diag * new_disp - stiff * neighbours(new_disp))
    partial_force = jnp.sum(inertia * new_disp, axis=1)
    force = sum_all(partial_force, "plate") * (8.0 / math.sqrt(total_cols * total_rows))
    every_force = gather_all(force, "storey").reshape(-1)
    every_shear = jnp.cumsum(every_force[::-1])[::-1]
    every_drift = jnp.cumsum(every_shear) / total_rows
    here_storey = lax.axis_index("storey")
    shear = lax.dynamic_slice_in_dim(every_shear, here_storey * rows, rows)
    drift = lax.dynamic_slice_in_dim(every_drift, here_storey * rows, rows)
    target = inertia * drift[:, None]
    adjoint = jnp.zeros_like(load) + correct(target, True)

    def adjoint_step(_, adjoint):
        resid = target - (diag * adjoint - neighbours(stiff * adjoint))
        return adjoint + correct(resid, True)

    adjoint = lax.fori_loop(0, ITERS - 1, adjoint_step, adjoint)
    partial_sums = damper_totals(damper_map, adjoint * new_disp, damper_coef.shape[0])
    sums = sum_all(partial_sums, "plate")
    grads = -CD * 64.0 / math.sqrt(rows * total_cols / damper_coef.shape[0]) * sums
    return (new_disp, adjoint, shear, grads)


def solution(mesh):
    return jax.shard_map(
        on_device,
        mesh=mesh,
        in_specs=(
            P("storey", "plate"),
            P("storey", "plate"),
            P("storey", "plate"),
            P("storey", "plate"),
            P(),
            P("storey", "plate"),
            P("storey"),
            P("storey", "plate"),
            P("storey", "plate"),
            P("storey"),
            P("storey", "plate"),
        ),
        out_specs=(P("storey", "plate"), P("storey", "plate"), P("storey"), P("storey")),
        check_vma=False,
    )
```
